32 devices in a mesh: group: 2 (over y), site: 4 (over z), inner: 4 (over x, core).
Axes of the slice: x: 2, y: 2, z: 4, core: 2. Of those that a mesh axis runs over, the one named last changes fastest.
Arguments:
- activations: bfloat16 [8, 384, 2560], P(('group', 'site'), None, 'inner'), parts along dimension 0, may hold values from -6 to 6
- out_grads: bfloat16 [8, 384, 1024], P(('group', 'site')), parts along dimension 0, may hold values from -6 to 6
- site_weights: bfloat16 [8, 1024, 2560], P(('group', 'site'), None, 'inner'), parts along dimension 0, may hold values from -6 to 6
Outputs:
- merged: float32 [2048, 2560], P(('group', 'site'), 'inner'), parts along dimension 0
The draws below stay inside these ranges and needn't reach their ends.
There are 2 independent parts, one for each index of `group`. The reference program is written for one: setup_inputs(seed, part) draws one part's arguments, and reference() takes and returns one part's arrays. A program takes and returns all parts, laid end to end along the dimension named above; each array names one. Nothing has to cross between parts.
All inputs are finite; a program needn't handle non-finite values.
Results may differ from the reference program's by a relative error of at most 0.0003.
Values sent between devices are 32-bit elements; how exact they have to be, the bound alone decides.
No kernel may reach another device: no remote copies, remote signals or barrier semaphores. Data moves between devices by JAX's collectives and lax.ppermute only.
A program may use at most 64 MiB of HBM per device.

```python
import jax
import jax.numpy as jnp
from jax import lax

DOUT = 1024
DIN = 2560
TOK = 384
ITERS = 4
SITES = 4


def with_spikes(array, key, source, target, parts, factor):
    def block_of(axis_at):
        return (jnp.arange(array.shape[axis_at]) // (array.shape[axis_at] // parts)).reshape((-1,) + (1,) * (array.ndim - 1 - axis_at))

    one_side = jax.random.permutation(key, parts)[block_of(target)]
    second = (block_of(target) + parts // 2) % parts
    return jnp.where((block_of(source) == one_side) | (block_of(source) == second), factor * array, array)


def level_of(key, shape, cuts, smallest, high):
    loudness, own = 1.0, jax.random.fold_in(key, 6)
    for position, blocks in cuts:
        steps = jnp.exp(jax.random.uniform(jax.random.fold_in(own, position), (blocks,), jnp.float32, smallest / len(cuts), high / len(cuts)))
        loudness = loudness * jnp.repeat(steps, shape[position] // blocks).reshape([-1 if axis == position else 1 for axis in range(len(shape))])
    return loudness


def bell_draw(key, extent, width, most, cuts=(), dtype=jnp.bfloat16):
    gain = level_of(key, extent, cuts, -0.22, 0.18) if cuts else 1.0
    drawn = jax.random.normal(key, extent, jnp.float32) * width * gain
    return jnp.minimum(jnp.maximum(drawn, -most), most).astype(dtype)


def noise_with(own_key, extent, deviation, reach, pieces, heavy, kind=jnp.bfloat16):
    array = deviation * jax.random.normal(own_key, extent, jnp.float32)
    if pieces:
        array = array * level_of(own_key, extent, pieces, -0.22, 0.18)
    return jnp.clip(with_spikes(array, jax.random.fold_in(own_key, 3), *heavy), -reach, reach).astype(kind)


def setup_inputs(seed: int = 0, part: int = 0) -> dict:
    key_of = jax.random.split(jax.random.key(seed), 4)
    part_splits = jax.random.split(jax.random.fold_in(key_of[3], part), 4)
    activations = bell_draw(part_splits[0], (SITES, TOK, DIN), 1.0, 6.0, ((0, 4), (2, 4)))
    out_grads = bell_draw(part_splits[1], (SITES, TOK, DOUT), 1.0, 6.0, ((0, 4),))
    site_weights = noise_with(part_splits[2], (SITES, DOUT, DIN), 1.0, 6.0, ((0, 4), (2, 4)), (0, 1, 4, 2.0))
    return dict(activations=activations, out_grads=out_grads, site_weights=site_weights)


damping = 1.0
highest = lax.Precision.HIGHEST


def site_term(matrix, inputs, grads):
    count = inputs.shape[0]
    in_float = inputs.astype(jnp.float32)
    grad_float = grads.astype(jnp.float32)
    left_prod = jnp.dot(grad_float, matrix, precision=highest)
    token_pair = jnp.dot(left_prod, in_float.T, precision=highest)
    mixed = jnp.dot(token_pair, in_float, precision=highest) / (count * count) + damping * left_prod / count
    return jnp.dot(grad_float.T, mixed, precision=highest)


def operator(matrix, activations, out_grads):
    def step(total, pair):
        return total + site_term(matrix, pair[0], pair[1]), None
    total, unused = lax.scan(step, jnp.zeros(matrix.shape, jnp.float32), (activations, out_grads))
    return total


def reference(activations, out_grads, site_weights):
    def step(total, triple):
        return total + site_term(triple[2].astype(jnp.float32), triple[0], triple[1]), None
    rhs, unused = lax.scan(step, jnp.zeros((DOUT, DIN), jnp.float32), (activations, out_grads, site_weights))
    merged = jnp.zeros((DOUT, DIN), jnp.float32)
    residual = rhs
    direction = rhs
    norm_now = jnp.sum(residual * residual)
    for count_step in range(ITERS):
        image = operator(direction, activations, out_grads)
        alpha = norm_now / jnp.sum(direction * image)
        merged = merged + alpha * direction
        residual = residual - alpha * image
        norm_next = jnp.sum(residual * residual)
        direction = residual + (norm_next / norm_now) * direction
        norm_now = norm_next
    return merged
```

```python
import jax
import jax.numpy as jnp
from jax import lax
from jax.sharding import PartitionSpec as P

ITERS = 4

damping = 1.0
f32 = jnp.float32
bf16 = jnp.bfloat16


def pieces(x):
    hi = lax.reduce_precision(x, exponent_bits=8, mantissa_bits=7)
    rest = x - hi
    mid = lax.reduce_precision(rest, exponent_bits=8, mantissa_bits=7)
    lo = rest - mid
    return hi.astype(bf16), mid.astype(bf16), lo.astype(bf16)


def exact_dot(spec, exact, value, exact_first=True):
    hi, mid, lo = pieces(value)

    def one(part):
        if exact_first:
            return jnp.einsum(spec, exact, part, preferred_element_type=f32)
        return jnp.einsum(spec, part, exact, preferred_element_type=f32)

    return one(hi) + (one(mid) + one(lo))


def site_gather(x):
    return lax.optimization_barrier(lax.all_gather(lax.optimization_barrier(x), "site"))


def inner_sum(x, size):
    if size & (size - 1):
        return lax.psum(x, "inner")
    bit = 1
    while bit < size:
        x = x + lax.ppermute(x, "inner", [(i, i ^ bit) for i in range(size)])
        bit *= 2
    return x


def per_device(activations, out_grads, site_weights):
    sites = lax.axis_size("site")
    inner = lax.axis_size("inner")
    me = lax.axis_index("site")
    inputs = activations[0]
    grads = out_grads[0]
    count = inputs.shape[0]
    rows = grads.shape[1] // sites

    every_input = (site_gather(inputs.astype(f32) * 2.0) * 0.5).astype(bf16)
    every_grad = (site_gather(grads.astype(f32) * 2.0) * 0.5).astype(bf16)

    def mixed_of(left, pair):
        return exact_dot("tu,uc->tc", inputs, pair, exact_first=False) / (count * count) + damping * left / count

    def token_pair(left):
        return inner_sum(exact_dot("tc,uc->tu", inputs, left, exact_first=False), inner)

    def image_of(mixed_all):
        return exact_dot("std,stc->dc", every_grad, mixed_all)

    left_w = jnp.dot(grads, site_weights[0], preferred_element_type=f32)
    mixed_w = mixed_of(left_w, token_pair(left_w))
    rhs = image_of(site_gather(mixed_w))

    def square_sum(x):
        return inner_sum(jnp.sum(x * x), inner)

    def apply_operator(direction):
        left_all = exact_dot("std,dc->stc", every_grad, direction)
        left_own = lax.dynamic_index_in_dim(left_all, me, 0, keepdims=False)
        pair_all = site_gather(token_pair(left_own))
        mixed_all = (
            exact_dot("stu,suc->stc", every_input, pair_all, exact_first=False) / (count * count)
            + damping * left_all / count
        )
        return image_of(mixed_all)

    merged = jnp.zeros_like(rhs)
    residual = rhs
    direction = rhs
    norm_now = square_sum(residual)
    for count_step in range(ITERS):
        image = apply_operator(direction)
        alpha = norm_now / inner_sum(jnp.sum(direction * image), inner)
        merged = merged + alpha * direction
        residual = residual - alpha * image
        norm_next = square_sum(residual)
        direction = residual + norm_next / norm_now * direction
        norm_now = norm_next
    return lax.dynamic_slice_in_dim(merged, me * rows, rows, 0)


def solution(mesh):
    return jax.shard_map(
        per_device,
        mesh=mesh,
        in_specs=(
            P(("group", "site"), None, "inner"),
            P(("group", "site"), None, None),
            P(("group", "site"), None, "inner"),
        ),
        out_specs=P(("group", "site"), "inner"),
        check_vma=False,
    )
```

```python
import jax
import jax.numpy as jnp
from jax import lax
from jax.sharding import PartitionSpec as P

ITERS = 4

damping = 1.0
f32 = jnp.float32
bf16 = jnp.bfloat16


def pieces(x):
    hi = lax.reduce_precision(x, exponent_bits=8, mantissa_bits=7)
    rest = x - hi
    mid = lax.reduce_precision(rest, exponent_bits=8, mantissa_bits=7)
    lo = rest - mid
    return hi.astype(bf16), mid.astype(bf16), lo.astype(bf16)


def exact_dot(spec, exact, value, exact_first=True):
    hi, mid, lo = pieces(value)

    def one(part):
        if exact_first:
            return jnp.einsum(spec, exact, part, preferred_element_type=f32)
        return jnp.einsum(spec, part, exact, preferred_element_type=f32)

    return one(hi) + (one(mid) + one(lo))


def site_gather(x):
    return lax.optimization_barrier(lax.all_gather(lax.optimization_barrier(x), "site"))


def inner_sum(x, size):
    if size & (size - 1):
        return lax.psum(x, "inner")
    bit = 1
    while bit < size:
        x = x + lax.ppermute(x, "inner", [(i, i ^ bit) for i in range(size)])
        bit *= 2
    return x


def halves(x, full, finish=lambda v: v):
    core = lax.axis_index("inner") % 2
    half = x.shape[1]
    other = lax.ppermute(x, "inner", [(i, i ^ 1) for i in range(lax.axis_size("inner"))])
    full = lax.dynamic_update_slice_in_dim(full, finish(x), core * half, 1)
    return lax.dynamic_update_slice_in_dim(full, finish(other), (1 - core) * half, 1)


def half_sum(x, size):
    core = lax.axis_index("inner") % 2
    half = x.shape[0] // 2
    mine = lax.dynamic_slice_in_dim(x, core * half, half, 0)
    theirs = lax.dynamic_slice_in_dim(x, (1 - core) * half, half, 0)
    part = mine + lax.ppermute(theirs, "inner", [(i, i ^ 1) for i in range(size)])
    bit = 2
    while bit < size:
        part = part + lax.ppermute(part, "inner", [(i, i ^ bit) for i in range(size)])
        bit *= 2
    return part


def per_device(activations, out_grads, site_weights):
    sites = lax.axis_size("site")
    inner = lax.axis_size("inner")
    me = lax.axis_index("site")
    inputs = activations[0]
    grads = out_grads[0]
    count = inputs.shape[0]
    rows = grads.shape[1] // sites

    every_input = (site_gather(inputs.astype(f32) * 2.0) * 0.5).astype(bf16)
    core = lax.axis_index("inner") % 2
    split = inner % 2 == 0 and count % 16 == 0
    if split:
        own_rows = lax.dynamic_slice_in_dim(grads, core * (count // 2), count // 2, 0)
        wide = site_gather(own_rows.astype(f32) * 2.0)
        every_grad = halves(wide, jnp.zeros((sites,) + grads.shape, bf16), lambda v: (v * 0.5).astype(bf16))
    else:
        every_grad = (site_gather(grads.astype(f32) * 2.0) * 0.5).astype(bf16)

    def mixed_of(left, pair):
        return exact_dot("tu,uc->tc", inputs, pair, exact_first=False) / (count * count) + damping * left / count

    def token_pair(left):
        return inner_sum(exact_dot("tc,uc->tu", inputs, left, exact_first=False), inner)

    def image_of(mixed_all):
        return exact_dot("std,stc->dc", every_grad, mixed_all)

    left_w = jnp.dot(grads, site_weights[0], preferred_element_type=f32)
    mixed_w = mixed_of(left_w, token_pair(left_w))
    rhs = image_of(site_gather(mixed_w))

    def square_sum(x):
        return inner_sum(jnp.sum(x * x), inner)

    def pair_gather(left):
        partial = exact_dot("tc,uc->tu", inputs, left, exact_first=False)
        if not split:
            return site_gather(inner_sum(partial, inner))
        return halves(site_gather(half_sum(partial, inner)), jnp.zeros((sites, count, count), f32))

    def apply_operator(direction):
        left_own = exact_dot("td,dc->tc", grads, direction)
        pair_all = pair_gather(left_own)
        left_all = exact_dot("std,dc->stc", every_grad, direction)
        mixed_all = (
            exact_dot("stu,suc->stc", every_input, pair_all, exact_first=False) / (count * count)
            + damping * left_all / count
        )
        return image_of(mixed_all)

    merged = jnp.zeros_like(rhs)
    residual = rhs
    direction = rhs
    norm_now = square_sum(residual)
    for count_step in range(ITERS):
        image = apply_operator(direction)
        alpha = norm_now / inner_sum(jnp.sum(direction * image), inner)
        merged = merged + alpha * direction
        residual = residual - alpha * image
        norm_next = square_sum(residual)
        direction = residual + norm_next / norm_now * direction
        norm_now = norm_next
    return lax.dynamic_slice_in_dim(merged, me * rows, rows, 0)


def solution(mesh):
    return jax.shard_map(
        per_device,
        mesh=mesh,
        in_specs=(
            P(("group", "site"), None, "inner"),
            P(("group", "site"), None, None),
            P(("group", "site"), None, "inner"),
        ),
        out_specs=P(("group", "site"), "inner"),
        check_vma=False,
    )
```

```python
import jax
import jax.numpy as jnp
from jax import lax
from jax.sharding import PartitionSpec as P

ITERS = 4

damping = 1.0
f32 = jnp.float32
bf16 = jnp.bfloat16


def pieces(x):
    hi = lax.reduce_precision(x, exponent_bits=8, mantissa_bits=7)
    rest = x - hi
    mid = lax.reduce_precision(rest, exponent_bits=8, mantissa_bits=7)
    lo = rest - mid
    return hi.astype(bf16), mid.astype(bf16), lo.astype(bf16)


def exact_dot(spec, exact, value, exact_first=True):
    hi, mid, lo = pieces(value)

    def one(part):
        if exact_first:
            return jnp.einsum(spec, exact, part, preferred_element_type=f32)
        return jnp.einsum(spec, part, exact, preferred_element_type=f32)

    return one(hi) + (one(mid) + one(lo))


def site_gather(x):
    return lax.optimization_barrier(lax.all_gather(lax.optimization_barrier(x), "site"))


def inner_sum(x, size):
    if size & (size - 1):
        return lax.psum(x, "inner")
    bit = 1
    while bit < size:
        x = x + lax.ppermute(x, "inner", [(i, i ^ bit) for i in range(size)])
        bit *= 2
    return x


def halves(x, full, finish=lambda v: v):
    core = lax.axis_index("inner") % 2
    half = x.shape[1]
    other = lax.ppermute(x, "inner", [(i, i ^ 1) for i in range(lax.axis_size("inner"))])
    full = lax.dynamic_update_slice_in_dim(full, finish(x), core * half, 1)
    return lax.dynamic_update_slice_in_dim(full, finish(other), (1 - core) * half, 1)


def half_sum(x, size):
    core = lax.axis_index("inner") % 2
    half = x.shape[0] // 2
    mine = lax.dynamic_slice_in_dim(x, core * half, half, 0)
    theirs = lax.dynamic_slice_in_dim(x, (1 - core) * half, half, 0)
    part = mine + lax.ppermute(theirs, "inner", [(i, i ^ 1) for i in range(size)])
    bit = 2
    while bit < size:
        part = part + lax.ppermute(part, "inner", [(i, i ^ bit) for i in range(size)])
        bit *= 2
    return part


def per_device(activations, out_grads, site_weights):
    sites = lax.axis_size("site")
    inner = lax.axis_size("inner")
    me = lax.axis_index("site")
    inputs = activations[0]
    grads = out_grads[0]
    count = inputs.shape[0]
    rows = grads.shape[1] // sites

    every_input = (site_gather(inputs.astype(f32) * 2.0) * 0.5).astype(bf16)
    core = lax.axis_index("inner") % 2
    split = inner % 2 == 0 and count % 16 == 0
    if split:
        own_rows = lax.dynamic_slice_in_dim(grads, core * (count // 2), count // 2, 0)
        wide = site_gather(own_rows.astype(f32) * 2.0)
        every_grad = halves(wide, jnp.zeros((sites,) + grads.shape, bf16), lambda v: (v * 0.5).astype(bf16))
    else:
        every_grad = (site_gather(grads.astype(f32) * 2.0) * 0.5).astype(bf16)

    def mixed_of(left, pair):
        return exact_dot("tu,uc->tc", inputs, pair, exact_first=False) / (count * count) + damping * left / count

    def token_pair(left):
        return inner_sum(exact_dot("tc,uc->tu", inputs, left, exact_first=False), inner)

    def image_of(mixed_all):
        return exact_dot("std,stc->dc", every_grad, mixed_all)

    left_w = jnp.dot(grads, site_weights[0], preferred_element_type=f32)
    mixed_w = mixed_of(left_w, token_pair(left_w))
    rhs = image_of(site_gather(mixed_w))

    def square_sum(x):
        return inner_sum(jnp.sum(x * x), inner)

    def pair_gather(left):
        partial = exact_dot("tc,uc->tu", inputs, left, exact_first=False)
        if not split:
            return site_gather(inner_sum(partial, inner))
        return halves(site_gather(half_sum(partial, inner)), jnp.zeros((sites, count, count), f32))

    def apply_operator(direction):
        left_own = exact_dot("td,dc->tc", grads, direction)
        pair_all = pair_gather(left_own)
        left_all = exact_dot("std,dc->stc", every_grad, direction)
        pair_all, left_all = lax.optimization_barrier((pair_all, left_all))
        mixed_all = (
            exact_dot("stu,suc->stc", every_input, pair_all, exact_first=False) / (count * count)
            + damping * left_all / count
        )
        return image_of(mixed_all)

    merged = jnp.zeros_like(rhs)
    residual = rhs
    direction = rhs
    norm_now = square_sum(residual)
    for count_step in range(ITERS):
        image = apply_operator(direction)
        alpha = norm_now / inner_sum(jnp.sum(direction * image), inner)
        merged = merged + alpha * direction
        residual = residual - alpha * image
        norm_next = square_sum(residual)
        direction = residual + norm_next / norm_now * direction
        norm_now = norm_next
    return lax.dynamic_slice_in_dim(merged, me * rows, rows, 0)


def solution(mesh):
    return jax.shard_map(
        per_device,
        mesh=mesh,
        in_specs=(
            P(("group", "site"), None, "inner"),
            P(("group", "site"), None, None),
            P(("group", "site"), None, "inner"),
        ),
        out_specs=P(("group", "site"), "inner"),
        check_vma=False,
    )
```

```python
import jax
import jax.numpy as jnp
from jax import lax
from jax.sharding import PartitionSpec as P

ITERS = 4

damping = 1.0
f32 = jnp.float32
bf16 = jnp.bfloat16


def pieces(x):
    hi = lax.reduce_precision(x, exponent_bits=8, mantissa_bits=7)
    rest = x - hi
    mid = lax.reduce_precision(rest, exponent_bits=8, mantissa_bits=7)
    lo = rest - mid
    return hi.astype(bf16), mid.astype(bf16), lo.astype(bf16)


def exact_dot(spec, exact, value, exact_first=True):
    hi, mid, lo = pieces(value)

    def one(part):
        if exact_first:
            return jnp.einsum(spec, exact, part, preferred_element_type=f32)
        return jnp.einsum(spec, part, exact, preferred_element_type=f32)

    return one(hi) + (one(mid) + one(lo))


def site_gather(x):
    return lax.optimization_barrier(lax.all_gather(lax.optimization_barrier(x), "site"))


def inner_sum(x, size):
    if size & (size - 1):
        return lax.psum(x, "inner")
    bit = 1
    while bit < size:
        x = x + lax.ppermute(x, "inner", [(i, i ^ bit) for i in range(size)])
        bit *= 2
    return x


def halves(x, full, finish=lambda v: v):
    core = lax.axis_index("inner") % 2
    half = x.shape[1]
    other = lax.ppermute(x, "inner", [(i, i ^ 1) for i in range(lax.axis_size("inner"))])
    full = lax.dynamic_update_slice_in_dim(full, finish(x), core * half, 1)
    return lax.dynamic_update_slice_in_dim(full, finish(other), (1 - core) * half, 1)


def half_sum(x, size):
    core = lax.axis_index("inner") % 2
    half = x.shape[0] // 2
    mine = lax.dynamic_slice_in_dim(x, core * half, half, 0)
    theirs = lax.dynamic_slice_in_dim(x, (1 - core) * half, half, 0)
    part = mine + lax.ppermute(theirs, "inner", [(i, i ^ 1) for i in range(size)])
    bit = 2
    while bit < size:
        part = part + lax.ppermute(part, "inner", [(i, i ^ bit) for i in range(size)])
        bit *= 2
    return part


def per_device(activations, out_grads, site_weights):
    sites = lax.axis_size("site")
    inner = lax.axis_size("inner")
    me = lax.axis_index("site")
    inputs = activations[0]
    grads = out_grads[0]
    count = inputs.shape[0]
    rows = grads.shape[1] // sites

    every_input = (site_gather(inputs.astype(f32) * 2.0) * 0.5).astype(bf16)
    core = lax.axis_index("inner") % 2
    split = inner % 2 == 0 and count % 16 == 0
    if split:
        own_rows = lax.dynamic_slice_in_dim(grads, core * (count // 2), count // 2, 0)
        wide = site_gather(own_rows.astype(f32) * 2.0)
        every_grad = halves(wide, jnp.zeros((sites,) + grads.shape, bf16), lambda v: (v * 0.5).astype(bf16))
    else:
        every_grad = (site_gather(grads.astype(f32) * 2.0) * 0.5).astype(bf16)

    def mixed_of(left, pair):
        return exact_dot("tu,uc->tc", inputs, pair, exact_first=False) / (count * count) + damping * left / count

    def token_pair(left):
        return inner_sum(exact_dot("tc,uc->tu", inputs, left, exact_first=False), inner)

    def image_of(mixed_all):
        return exact_dot("std,stc->dc", every_grad, mixed_all)

    left_w = jnp.dot(grads, site_weights[0], preferred_element_type=f32)
    mixed_w = mixed_of(left_w, token_pair(left_w))
    rhs = image_of(site_gather(mixed_w))

    def square_sum(x):
        return inner_sum(jnp.sum(x * x), inner)

    def pair_sum(left, scalar):
        partial = exact_dot("tc,uc->tu", inputs, left, exact_first=False)
        extra = jnp.full((8, count), scalar, f32)
        if not split:
            total = inner_sum(jnp.concatenate([partial, extra]), inner)
            return total[:count], total[count, 0]
        half = count // 2
        mine = jnp.concatenate([lax.dynamic_slice_in_dim(partial, core * half, half, 0), extra])
        theirs = jnp.concatenate([lax.dynamic_slice_in_dim(partial, (1 - core) * half, half, 0), extra])
        part = mine + lax.ppermute(theirs, "inner", [(i, i ^ 1) for i in range(inner)])
        bit = 2
        while bit < inner:
            part = part + lax.ppermute(part, "inner", [(i, i ^ bit) for i in range(inner)])
            bit *= 2
        return part[:half], part[half, 0]

    def pair_spread(pair_part):
        if not split:
            return site_gather(pair_part)
        return halves(site_gather(pair_part), jnp.zeros((sites, count, count), f32))

    def apply_operator(pair_part, direction):
        pair_all = pair_spread(pair_part)
        left_all = exact_dot("std,dc->stc", every_grad, direction)
        pair_all, left_all = lax.optimization_barrier((pair_all, left_all))
        mixed_all = (
            exact_dot("stu,suc->stc", every_input, pair_all, exact_first=False) / (count * count)
            + damping * left_all / count
        )
        return image_of(mixed_all)

    merged = jnp.zeros_like(rhs)
    residual = rhs
    direction = rhs
    pair_part, norm_now = pair_sum(exact_dot("td,dc->tc", grads, rhs), jnp.sum(rhs * rhs))
    for count_step in range(ITERS):
        if count_step:
            pair_r, norm_next = pair_sum(exact_dot("td,dc->tc", grads, residual), jnp.sum(residual * residual))
            beta = norm_next / norm_now
            pair_part = pair_r + beta * pair_part
            direction = residual + beta * direction
            norm_now = norm_next
        image = apply_operator(pair_part, direction)
        alpha = norm_now / inner_sum(jnp.sum(direction * image), inner)
        merged = merged + alpha * direction
        residual = residual - alpha * image
    norm_next = square_sum(residual)
    direction = residual + norm_next / norm_now * direction
    return lax.dynamic_slice_in_dim(merged, me * rows, rows, 0)


def solution(mesh):
    return jax.shard_map(
        per_device,
        mesh=mesh,
        in_specs=(
            P(("group", "site"), None, "inner"),
            P(("group", "site"), None, None),
            P(("group", "site"), None, "inner"),
        ),
        out_specs=P(("group", "site"), "inner"),
        check_vma=False,
    )
```

```python
import jax
import jax.numpy as jnp
from jax import lax
from jax.sharding import PartitionSpec as P

ITERS = 4

damping = 1.0
f32 = jnp.float32
bf16 = jnp.bfloat16


def pieces(x):
    hi = lax.reduce_precision(x, exponent_bits=8, mantissa_bits=7)
    rest = x - hi
    mid = lax.reduce_precision(rest, exponent_bits=8, mantissa_bits=7)
    lo = rest - mid
    return hi.astype(bf16), mid.astype(bf16), lo.astype(bf16)


def exact_dot(spec, exact, value, exact_first=True):
    hi, mid, lo = pieces(value)

    def one(part):
        if exact_first:
            return jnp.einsum(spec, exact, part, preferred_element_type=f32)
        return jnp.einsum(spec, part, exact, preferred_element_type=f32)

    return one(hi) + (one(mid) + one(lo))


def site_gather(x):
    return lax.optimization_barrier(lax.all_gather(lax.optimization_barrier(x), "site"))


def line_gather(x):
    sites = lax.axis_size("site")
    me = lax.axis_index("site")
    out = lax.dynamic_update_slice_in_dim(jnp.zeros((sites,) + x.shape, x.dtype), x[None], me, 0)
    right = left = x
    for step in range(1, sites):
        right = lax.ppermute(right, "site", [(i, i + 1) for i in range(sites - 1)])
        left = lax.ppermute(left, "site", [(i + 1, i) for i in range(sites - 1)])
        for block, at in ((right, (me - step) % sites), (left, (me + step) % sites)):
            now = lax.dynamic_index_in_dim(out, at, 0)
            out = lax.dynamic_update_slice_in_dim(out, now + block[None], at, 0)
    return out


def inner_sum(x, size):
    if size & (size - 1):
        return lax.psum(x, "inner")
    bit = 1
    while bit < size:
        x = x + lax.ppermute(x, "inner", [(i, i ^ bit) for i in range(size)])
        bit *= 2
    return x


def halves(x, full, finish=lambda v: v):
    core = lax.axis_index("inner") % 2
    half = x.shape[1]
    other = lax.ppermute(x, "inner", [(i, i ^ 1) for i in range(lax.axis_size("inner"))])
    full = lax.dynamic_update_slice_in_dim(full, finish(x), core * half, 1)
    return lax.dynamic_update_slice_in_dim(full, finish(other), (1 - core) * half, 1)


def half_sum(x, size):
    core = lax.axis_index("inner") % 2
    half = x.shape[0] // 2
    mine = lax.dynamic_slice_in_dim(x, core * half, half, 0)
    theirs = lax.dynamic_slice_in_dim(x, (1 - core) * half, half, 0)
    part = mine + lax.ppermute(theirs, "inner", [(i, i ^ 1) for i in range(size)])
    bit = 2
    while bit < size:
        part = part + lax.ppermute(part, "inner", [(i, i ^ bit) for i in range(size)])
        bit *= 2
    return part


def per_device(activations, out_grads, site_weights):
    sites = lax.axis_size("site")
    inner = lax.axis_size("inner")
    me = lax.axis_index("site")
    inputs = activations[0]
    grads = out_grads[0]
    count = inputs.shape[0]
    rows = grads.shape[1] // sites

    every_input = (line_gather(inputs.astype(f32) * 2.0) * 0.5).astype(bf16)
    core = lax.axis_index("inner") % 2
    split = inner % 2 == 0 and count % 16 == 0
    if split:
        own_rows = lax.dynamic_slice_in_dim(grads, core * (count // 2), count // 2, 0)
        wide = site_gather(own_rows.astype(f32) * 2.0)
        every_grad = halves(wide, jnp.zeros((sites,) + grads.shape, bf16), lambda v: (v * 0.5).astype(bf16))
    else:
        every_grad = (site_gather(grads.astype(f32) * 2.0) * 0.5).astype(bf16)

    def mixed_of(left, pair):
        return exact_dot("tu,uc->tc", inputs, pair, exact_first=False) / (count * count) + damping * left / count

    def token_pair(left):
        return inner_sum(exact_dot("tc,uc->tu", inputs, left, exact_first=False), inner)

    def image_of(mixed_all):
        return exact_dot("std,stc->dc", every_grad, mixed_all)

    left_w = jnp.dot(grads, site_weights[0], preferred_element_type=f32)
    mixed_w = mixed_of(left_w, token_pair(left_w))
    rhs = image_of(site_gather(mixed_w))

    def square_sum(x):
        return inner_sum(jnp.sum(x * x), inner)

    def pair_sum(left, scalar):
        partial = exact_dot("tc,uc->tu", inputs, left, exact_first=False)
        extra = jnp.full((8, count), scalar, f32)
        if not split:
            total = inner_sum(jnp.concatenate([partial, extra]), inner)
            return total[:count], total[count, 0]
        half = count // 2
        mine = jnp.concatenate([lax.dynamic_slice_in_dim(partial, core * half, half, 0), extra])
        theirs = jnp.concatenate([lax.dynamic_slice_in_dim(partial, (1 - core) * half, half, 0), extra])
        part = mine + lax.ppermute(theirs, "inner", [(i, i ^ 1) for i in range(inner)])
        bit = 2
        while bit < inner:
            part = part + lax.ppermute(part, "inner", [(i, i ^ bit) for i in range(inner)])
            bit *= 2
        return part[:half], part[half, 0]

    def pair_spread(pair_part):
        if not split:
            return site_gather(pair_part)
        return halves(site_gather(pair_part), jnp.zeros((sites, count, count), f32))

    def apply_operator(pair_part, direction):
        pair_all = pair_spread(pair_part)
        left_all = exact_dot("std,dc->stc", every_grad, direction)
        pair_all, left_all = lax.optimization_barrier((pair_all, left_all))
        mixed_all = (
            exact_dot("stu,suc->stc", every_input, pair_all, exact_first=False) / (count * count)
            + damping * left_all / count
        )
        return image_of(mixed_all)

    merged = jnp.zeros_like(rhs)
    residual = rhs
    direction = rhs
    pair_part, norm_now = pair_sum(exact_dot("td,dc->tc", grads, rhs), jnp.sum(rhs * rhs))
    for count_step in range(ITERS):
        if count_step:
            pair_r, norm_next = pair_sum(exact_dot("td,dc->tc", grads, residual), jnp.sum(residual * residual))
            beta = norm_next / norm_now
            pair_part = pair_r + beta * pair_part
            direction = residual + beta * direction
            norm_now = norm_next
        image = apply_operator(pair_part, direction)
        alpha = norm_now / inner_sum(jnp.sum(direction * image), inner)
        merged = merged + alpha * direction
        residual = residual - alpha * image
    norm_next = square_sum(residual)
    direction = residual + norm_next / norm_now * direction
    return lax.dynamic_slice_in_dim(merged, me * rows, rows, 0)


def solution(mesh):
    return jax.shard_map(
        per_device,
        mesh=mesh,
        in_specs=(
            P(("group", "site"), None, "inner"),
            P(("group", "site"), None, None),
            P(("group", "site"), None, "inner"),
        ),
        out_specs=P(("group", "site"), "inner"),
        check_vma=False,
    )
```

```python
import jax
import jax.numpy as jnp
from jax import lax
from jax.sharding import PartitionSpec as P

ITERS = 4

damping = 1.0
f32 = jnp.float32
bf16 = jnp.bfloat16


def pieces(x):
    hi = lax.reduce_precision(x, exponent_bits=8, mantissa_bits=7)
    rest = x - hi
    mid = lax.reduce_precision(rest, exponent_bits=8, mantissa_bits=7)
    lo = rest - mid
    return hi.astype(bf16), mid.astype(bf16), lo.astype(bf16)


def exact_dot(spec, exact, value, exact_first=True):
    hi, mid, lo = pieces(value)

    def one(part):
        if exact_first:
            return jnp.einsum(spec, exact, part, preferred_element_type=f32)
        return jnp.einsum(spec, part, exact, preferred_element_type=f32)

    return one(hi) + (one(mid) + one(lo))


def site_gather(x):
    return lax.optimization_barrier(lax.all_gather(lax.optimization_barrier(x), "site"))


def line_gather(x):
    sites = lax.axis_size("site")
    me = lax.axis_index("site")
    out = lax.dynamic_update_slice_in_dim(jnp.zeros((sites,) + x.shape, x.dtype), x[None], me, 0)
    right = left = x
    for step in range(1, sites):
        right = lax.ppermute(right, "site", [(i, i + 1) for i in range(sites - 1)])
        left = lax.ppermute(left, "site", [(i + 1, i) for i in range(sites - 1)])
        for block, at in ((right, (me - step) % sites), (left, (me + step) % sites)):
            now = lax.dynamic_index_in_dim(out, at, 0)
            out = lax.dynamic_update_slice_in_dim(out, now + block[None], at, 0)
    return out


def inner_sum(x, size):
    if size & (size - 1):
        return lax.psum(x, "inner")
    bit = 1
    while bit < size:
        x = x + lax.ppermute(x, "inner", [(i, i ^ bit) for i in range(size)])
        bit *= 2
    return x


def halves(x, finish=lambda v: v):
    other = lax.ppermute(x, "inner", [(i, i ^ 1) for i in range(lax.axis_size("inner"))])
    return jnp.concatenate([finish(x), finish(other)], axis=1)


def half_sum(x, size):
    core = lax.axis_index("inner") % 2
    half = x.shape[0] // 2
    mine = lax.dynamic_slice_in_dim(x, core * half, half, 0)
    theirs = lax.dynamic_slice_in_dim(x, (1 - core) * half, half, 0)
    part = mine + lax.ppermute(theirs, "inner", [(i, i ^ 1) for i in range(size)])
    bit = 2
    while bit < size:
        part = part + lax.ppermute(part, "inner", [(i, i ^ bit) for i in range(size)])
        bit *= 2
    return part


def per_device(activations, out_grads, site_weights):
    sites = lax.axis_size("site")
    inner = lax.axis_size("inner")
    me = lax.axis_index("site")
    inputs = activations[0]
    grads = out_grads[0]
    count = inputs.shape[0]
    rows = grads.shape[1] // sites

    every_input = (line_gather(inputs.astype(f32) * 2.0) * 0.5).astype(bf16)
    core = lax.axis_index("inner") % 2
    split = inner % 2 == 0 and count % 16 == 0
    if split:
        own_rows = lax.dynamic_slice_in_dim(grads, core * (count // 2), count // 2, 0)
        wide = site_gather(own_rows.astype(f32) * 2.0)
        every_grad = halves(wide, lambda v: (v * 0.5).astype(bf16))
    else:
        every_grad = (site_gather(grads.astype(f32) * 2.0) * 0.5).astype(bf16)

    def mixed_of(left, pair):
        return exact_dot("tu,uc->tc", inputs, pair, exact_first=False) / (count * count) + damping * left / count

    def token_pair(left):
        return inner_sum(exact_dot("tc,uc->tu", inputs, left, exact_first=False), inner)

    def image_of(mixed_all):
        return exact_dot("std,stc->dc", every_grad, mixed_all)

    left_w = jnp.dot(grads, site_weights[0], preferred_element_type=f32)
    mixed_w = mixed_of(left_w, token_pair(left_w))
    mixed_w_all = site_gather(mixed_w)
    if split:
        half = count // 2
        turned = jnp.concatenate([mixed_w_all[:, half:], mixed_w_all[:, :half]], axis=1)
        mixed_w_all = jnp.where(core == 0, mixed_w_all, turned)
    rhs = image_of(mixed_w_all)

    def square_sum(x):
        return inner_sum(jnp.sum(x * x), inner)

    def pair_sum(left, scalar):
        partial = exact_dot("tc,uc->tu", inputs, left, exact_first=False)
        extra = jnp.full((8, count), scalar, f32)
        if not split:
            total = inner_sum(jnp.concatenate([partial, extra]), inner)
            return total[:count], total[count, 0]
        half = count // 2
        mine = jnp.concatenate([lax.dynamic_slice_in_dim(partial, core * half, half, 0), extra])
        theirs = jnp.concatenate([lax.dynamic_slice_in_dim(partial, (1 - core) * half, half, 0), extra])
        part = mine + lax.ppermute(theirs, "inner", [(i, i ^ 1) for i in range(inner)])
        bit = 2
        while bit < inner:
            part = part + lax.ppermute(part, "inner", [(i, i ^ bit) for i in range(inner)])
            bit *= 2
        return part[:half], part[half, 0]

    def pair_spread(pair_part):
        if not split:
            return site_gather(pair_part)
        return halves(site_gather(pair_part))

    def apply_operator(pair_part, direction):
        pair_all = pair_spread(pair_part)
        left_all = exact_dot("std,dc->stc", every_grad, direction)
        pair_all, left_all = lax.optimization_barrier((pair_all, left_all))
        mixed_all = (
            exact_dot("stu,suc->stc", every_input, pair_all, exact_first=False) / (count * count)
            + damping * left_all / count
        )
        return image_of(mixed_all)

    merged = jnp.zeros_like(rhs)
    residual = rhs
    direction = rhs
    pair_part, norm_now = pair_sum(exact_dot("td,dc->tc", grads, rhs), jnp.sum(rhs * rhs))
    for count_step in range(ITERS):
        if count_step:
            pair_r, norm_next = pair_sum(exact_dot("td,dc->tc", grads, residual), jnp.sum(residual * residual))
            beta = norm_next / norm_now
            pair_part = pair_r + beta * pair_part
            direction = residual + beta * direction
            norm_now = norm_next
        image = apply_operator(pair_part, direction)
        alpha = norm_now / inner_sum(jnp.sum(direction * image), inner)
        merged = merged + alpha * direction
        residual = residual - alpha * image
    norm_next = square_sum(residual)
    direction = residual + norm_next / norm_now * direction
    return lax.dynamic_slice_in_dim(merged, me * rows, rows, 0)


def solution(mesh):
    return jax.shard_map(
        per_device,
        mesh=mesh,
        in_specs=(
            P(("group", "site"), None, "inner"),
            P(("group", "site"), None, None),
            P(("group", "site"), None, "inner"),
        ),
        out_specs=P(("group", "site"), "inner"),
        check_vma=False,
    )
```

```python
import jax
import jax.numpy as jnp
from jax import lax
from jax.sharding import PartitionSpec as P

ITERS = 4

damping = 1.0
f32 = jnp.float32
bf16 = jnp.bfloat16


def pieces(x):
    hi = lax.reduce_precision(x, exponent_bits=8, mantissa_bits=7)
    rest = x - hi
    mid = lax.reduce_precision(rest, exponent_bits=8, mantissa_bits=7)
    lo = rest - mid
    return hi.astype(bf16), mid.astype(bf16), lo.astype(bf16)


def exact_dot(spec, exact, value, exact_first=True):
    hi, mid, lo = pieces(value)

    def one(part):
        if exact_first:
            return jnp.einsum(spec, exact, part, preferred_element_type=f32)
        return jnp.einsum(spec, part, exact, preferred_element_type=f32)

    return one(hi) + (one(mid) + one(lo))


def site_gather(x):
    return lax.optimization_barrier(lax.all_gather(lax.optimization_barrier(x), "site"))


def line_gather(x):
    sites = lax.axis_size("site")
    me = lax.axis_index("site")
    out = lax.dynamic_update_slice_in_dim(jnp.zeros((sites,) + x.shape, x.dtype), x[None], me, 0)
    right = left = x
    for step in range(1, sites):
        right = lax.ppermute(right, "site", [(i, i + 1) for i in range(sites - 1)])
        left = lax.ppermute(left, "site", [(i + 1, i) for i in range(sites - 1)])
        for block, at in ((right, (me - step) % sites), (left, (me + step) % sites)):
            now = lax.dynamic_index_in_dim(out, at, 0)
            out = lax.dynamic_update_slice_in_dim(out, now + block[None], at, 0)
    return out


def inner_sum(x, size):
    if size & (size - 1):
        return lax.psum(x, "inner")
    bit = 1
    while bit < size:
        x = x + lax.ppermute(x, "inner", [(i, i ^ bit) for i in range(size)])
        bit *= 2
    return x


def halves(x, finish=lambda v: v):
    other = lax.ppermute(x, "inner", [(i, i ^ 1) for i in range(lax.axis_size("inner"))])
    return jnp.concatenate([finish(x), finish(other)], axis=1)


def half_sum(x, size):
    core = lax.axis_index("inner") % 2
    half = x.shape[0] // 2
    mine = lax.dynamic_slice_in_dim(x, core * half, half, 0)
    theirs = lax.dynamic_slice_in_dim(x, (1 - core) * half, half, 0)
    part = mine + lax.ppermute(theirs, "inner", [(i, i ^ 1) for i in range(size)])
    bit = 2
    while bit < size:
        part = part + lax.ppermute(part, "inner", [(i, i ^ bit) for i in range(size)])
        bit *= 2
    return part


def per_device(activations, out_grads, site_weights):
    sites = lax.axis_size("site")
    inner = lax.axis_size("inner")
    me = lax.axis_index("site")
    inputs = activations[0]
    grads = out_grads[0]
    count = inputs.shape[0]
    rows = grads.shape[1] // sites

    every_input = (line_gather(inputs.astype(f32) * 2.0) * 0.5).astype(bf16)
    core = lax.axis_index("inner") % 2
    split = inner % 2 == 0 and count % 16 == 0
    if split:
        own_rows = lax.dynamic_slice_in_dim(grads, core * (count // 2), count // 2, 0)
        wide = site_gather(own_rows.astype(f32) * 2.0)
        every_grad = halves(wide, lambda v: (v * 0.5).astype(bf16))
    else:
        every_grad = (site_gather(grads.astype(f32) * 2.0) * 0.5).astype(bf16)

    def mixed_of(left, pair):
        return exact_dot("tu,uc->tc", inputs, pair, exact_first=False) / (count * count) + damping * left / count

    def token_pair(left):
        return inner_sum(exact_dot("tc,uc->tu", inputs, left, exact_first=False), inner)

    def image_of(mixed_all):
        return exact_dot("std,stc->dc", every_grad, mixed_all)

    left_w = jnp.dot(grads, site_weights[0], preferred_element_type=f32)
    mixed_w = mixed_of(left_w, token_pair(left_w))
    mixed_w_all = site_gather(mixed_w)
    if split:
        half = count // 2
        turned = jnp.concatenate([mixed_w_all[:, half:], mixed_w_all[:, :half]], axis=1)
        mixed_w_all = jnp.where(core == 0, mixed_w_all, turned)
    rhs = image_of(mixed_w_all)

    def square_sum(x):
        return inner_sum(jnp.sum(x * x), inner)

    def pair_sum(left, scalar):
        partial = exact_dot("tc,uc->tu", inputs, left, exact_first=False)
        extra = jnp.full((8, count), scalar, f32)
        if not split:
            total = inner_sum(jnp.concatenate([partial, extra]), inner)
            return total[:count], total[count, 0]
        half = count // 2
        mine = jnp.concatenate([lax.dynamic_slice_in_dim(partial, core * half, half, 0), extra])
        theirs = jnp.concatenate([lax.dynamic_slice_in_dim(partial, (1 - core) * half, half, 0), extra])
        part = mine + lax.ppermute(theirs, "inner", [(i, i ^ 1) for i in range(inner)])
        bit = 2
        while bit < inner:
            part = part + lax.ppermute(part, "inner", [(i, i ^ bit) for i in range(inner)])
            bit *= 2
        return part[:half], part[half, 0]

    def pair_spread(pair_part):
        if not split:
            return site_gather(pair_part)
        return halves(site_gather(pair_part))

    def apply_operator(pair_part, left_all):
        pair_all = pair_spread(pair_part)
        mixed_all = (
            exact_dot("stu,suc->stc", every_input, pair_all, exact_first=False) / (count * count)
            + damping * left_all / count
        )
        return image_of(mixed_all)

    merged = jnp.zeros_like(rhs)
    residual = rhs
    direction = rhs
    pair_part, norm_now = pair_sum(exact_dot("td,dc->tc", grads, rhs), jnp.sum(rhs * rhs))
    left_all = exact_dot("std,dc->stc", every_grad, rhs)
    for count_step in range(ITERS):
        if count_step:
            left_r = exact_dot("std,dc->stc", every_grad, residual)
            pair_r, norm_next = pair_sum(exact_dot("td,dc->tc", grads, residual), jnp.sum(residual * residual))
            beta = norm_next / norm_now
            pair_part = pair_r + beta * pair_part
            left_all = left_r + beta * left_all
            direction = residual + beta * direction
            norm_now = norm_next
        image = apply_operator(pair_part, left_all)
        alpha = norm_now / inner_sum(jnp.sum(direction * image), inner)
        merged = merged + alpha * direction
        residual = residual - alpha * image
    norm_next = square_sum(residual)
    direction = residual + norm_next / norm_now * direction
    return lax.dynamic_slice_in_dim(merged, me * rows, rows, 0)


def solution(mesh):
    return jax.shard_map(
        per_device,
        mesh=mesh,
        in_specs=(
            P(("group", "site"), None, "inner"),
            P(("group", "site"), None, None),
            P(("group", "site"), None, "inner"),
        ),
        out_specs=P(("group", "site"), "inner"),
        check_vma=False,
    )
```

```python
import jax
import jax.numpy as jnp
from jax import lax
from jax.sharding import PartitionSpec as P

ITERS = 4

damping = 1.0
f32 = jnp.float32
bf16 = jnp.bfloat16


def pieces(x):
    hi = lax.reduce_precision(x, exponent_bits=8, mantissa_bits=7)
    rest = x - hi
    mid = lax.reduce_precision(rest, exponent_bits=8, mantissa_bits=7)
    lo = rest - mid
    return hi.astype(bf16), mid.astype(bf16), lo.astype(bf16)


def exact_dot(spec, exact, value, exact_first=True):
    hi, mid, lo = pieces(value)

    def one(part):
        if exact_first:
            return jnp.einsum(spec, exact, part, preferred_element_type=f32)
        return jnp.einsum(spec, part, exact, preferred_element_type=f32)

    return one(hi) + (one(mid) + one(lo))


def site_gather(x):
    return lax.optimization_barrier(lax.all_gather(lax.optimization_barrier(x), "site"))


def line_gather(x):
    sites = lax.axis_size("site")
    me = lax.axis_index("site")
    out = lax.dynamic_update_slice_in_dim(jnp.zeros((sites,) + x.shape, x.dtype), x[None], me, 0)
    right = left = x
    for step in range(1, sites):
        right = lax.ppermute(right, "site", [(i, i + 1) for i in range(sites - 1)])
        left = lax.ppermute(left, "site", [(i + 1, i) for i in range(sites - 1)])
        for block, at in ((right, (me - step) % sites), (left, (me + step) % sites)):
            now = lax.dynamic_index_in_dim(out, at, 0)
            out = lax.dynamic_update_slice_in_dim(out, now + block[None], at, 0)
    return out


def inner_sum(x, size):
    if size & (size - 1):
        return lax.psum(x, "inner")
    bit = 1
    while bit < size:
        x = x + lax.ppermute(x, "inner", [(i, i ^ bit) for i in range(size)])
        bit *= 2
    return x


def halves(x, finish=lambda v: v):
    other = lax.ppermute(x, "inner", [(i, i ^ 1) for i in range(lax.axis_size("inner"))])
    return jnp.concatenate([finish(x), finish(other)], axis=1)


def half_sum(x, size):
    core = lax.axis_index("inner") % 2
    half = x.shape[0] // 2
    mine = lax.dynamic_slice_in_dim(x, core * half, half, 0)
    theirs = lax.dynamic_slice_in_dim(x, (1 - core) * half, half, 0)
    part = mine + lax.ppermute(theirs, "inner", [(i, i ^ 1) for i in range(size)])
    bit = 2
    while bit < size:
        part = part + lax.ppermute(part, "inner", [(i, i ^ bit) for i in range(size)])
        bit *= 2
    return part


def per_device(activations, out_grads, site_weights):
    sites = lax.axis_size("site")
    inner = lax.axis_size("inner")
    me = lax.axis_index("site")
    inputs = activations[0]
    grads = out_grads[0]
    count = inputs.shape[0]
    rows = grads.shape[1] // sites

    every_input = (line_gather(inputs.astype(f32) * 2.0) * 0.5).astype(bf16)
    core = lax.axis_index("inner") % 2
    split = inner % 2 == 0 and count % 16 == 0
    if split:
        own_rows = lax.dynamic_slice_in_dim(grads, core * (count // 2), count // 2, 0)
        wide = site_gather(own_rows.astype(f32) * 2.0)
        every_grad = halves(wide, lambda v: (v * 0.5).astype(bf16))
    else:
        every_grad = (site_gather(grads.astype(f32) * 2.0) * 0.5).astype(bf16)

    def mixed_of(left, pair):
        return exact_dot("tu,uc->tc", inputs, pair, exact_first=False) / (count * count) + damping * left / count

    def token_pair(left):
        return inner_sum(exact_dot("tc,uc->tu", inputs, left, exact_first=False), inner)

    def image_of(mixed_all):
        return exact_dot("std,stc->dc", every_grad, mixed_all)

    left_w = jnp.dot(grads, site_weights[0], preferred_element_type=f32)
    mixed_w = mixed_of(left_w, token_pair(left_w))
    mixed_w_all = site_gather(mixed_w)
    if split:
        half = count // 2
        turned = jnp.concatenate([mixed_w_all[:, half:], mixed_w_all[:, :half]], axis=1)
        mixed_w_all = jnp.where(core == 0, mixed_w_all, turned)
    rhs = image_of(mixed_w_all)

    def square_sum(x):
        return inner_sum(jnp.sum(x * x), inner)

    def pair_sum(left, scalar):
        partial = exact_dot("tc,uc->tu", inputs, left, exact_first=False)
        extra = jnp.full((8, count), scalar, f32)
        if not split:
            total = inner_sum(jnp.concatenate([partial, extra]), inner)
            return total[:count], total[count, 0]
        half = count // 2
        mine = jnp.concatenate([lax.dynamic_slice_in_dim(partial, core * half, half, 0), extra])
        theirs = jnp.concatenate([lax.dynamic_slice_in_dim(partial, (1 - core) * half, half, 0), extra])
        part = mine + lax.ppermute(theirs, "inner", [(i, i ^ 1) for i in range(inner)])
        bit = 2
        while bit < inner:
            part = part + lax.ppermute(part, "inner", [(i, i ^ bit) for i in range(inner)])
            bit *= 2
        return part[:half], part[half, 0]

    def pair_spread(pair_part):
        if not split:
            return site_gather(pair_part)
        return halves(site_gather(pair_part))

    def apply_operator(pair_part, direction):
        pair_all = pair_spread(pair_part)
        left_all = exact_dot("std,dc->stc", every_grad, direction)
        pair_all, left_all = lax.optimization_barrier((pair_all, left_all))
        mixed_all = (
            exact_dot("stu,suc->stc", every_input, pair_all, exact_first=False) / (count * count)
            + damping * left_all / count
        )
        return image_of(mixed_all), inner_sum(jnp.sum(left_all * mixed_all), inner)

    merged = jnp.zeros_like(rhs)
    residual = rhs
    direction = rhs
    pair_part, norm_now = pair_sum(exact_dot("td,dc->tc", grads, rhs), jnp.sum(rhs * rhs))
    for count_step in range(ITERS):
        if count_step:
            pair_r, norm_next = pair_sum(exact_dot("td,dc->tc", grads, residual), jnp.sum(residual * residual))
            beta = norm_next / norm_now
            pair_part = pair_r + beta * pair_part
            direction = residual + beta * direction
            norm_now = norm_next
        image, curvature = apply_operator(pair_part, direction)
        alpha = norm_now / curvature
        merged = merged + alpha * direction
        residual = residual - alpha * image
    norm_next = square_sum(residual)
    direction = residual + norm_next / norm_now * direction
    return lax.dynamic_slice_in_dim(merged, me * rows, rows, 0)


def solution(mesh):
    return jax.shard_map(
        per_device,
        mesh=mesh,
        in_specs=(
            P(("group", "site"), None, "inner"),
            P(("group", "site"), None, None),
            P(("group", "site"), None, "inner"),
        ),
        out_specs=P(("group", "site"), "inner"),
        check_vma=False,
    )
```

```python
import jax
import jax.numpy as jnp
from jax import lax
from jax.sharding import PartitionSpec as P

ITERS = 4

damping = 1.0
f32 = jnp.float32
bf16 = jnp.bfloat16


def pieces(x):
    hi = lax.reduce_precision(x, exponent_bits=8, mantissa_bits=7)
    rest = x - hi
    mid = lax.reduce_precision(rest, exponent_bits=8, mantissa_bits=7)
    lo = rest - mid
    return hi.astype(bf16), mid.astype(bf16), lo.astype(bf16)


def exact_dot(spec, exact, value, exact_first=True):
    hi, mid, lo = pieces(value)

    def one(part):
        if exact_first:
            return jnp.einsum(spec, exact, part, preferred_element_type=f32)
        return jnp.einsum(spec, part, exact, preferred_element_type=f32)

    return one(hi) + (one(mid) + one(lo))


def site_gather(x):
    return lax.optimization_barrier(lax.all_gather(lax.optimization_barrier(x), "site"))


def line_gather(x):
    sites = lax.axis_size("site")
    me = lax.axis_index("site")
    out = lax.dynamic_update_slice_in_dim(jnp.zeros((sites,) + x.shape, x.dtype), x[None], me, 0)
    right = left = x
    for step in range(1, sites):
        right = lax.ppermute(right, "site", [(i, i + 1) for i in range(sites - 1)])
        left = lax.ppermute(left, "site", [(i + 1, i) for i in range(sites - 1)])
        for block, at in ((right, (me - step) % sites), (left, (me + step) % sites)):
            now = lax.dynamic_index_in_dim(out, at, 0)
            out = lax.dynamic_update_slice_in_dim(out, now + block[None], at, 0)
    return out


def inner_sum(x, size):
    if size & (size - 1):
        return lax.psum(x, "inner")
    bit = 1
    while bit < size:
        x = x + lax.ppermute(x, "inner", [(i, i ^ bit) for i in range(size)])
        bit *= 2
    return x


def halves(x, finish=lambda v: v):
    other = lax.ppermute(x, "inner", [(i, i ^ 1) for i in range(lax.axis_size("inner"))])
    return jnp.concatenate([finish(x), finish(other)], axis=1)


def half_sum(x, size):
    core = lax.axis_index("inner") % 2
    half = x.shape[0] // 2
    mine = lax.dynamic_slice_in_dim(x, core * half, half, 0)
    theirs = lax.dynamic_slice_in_dim(x, (1 - core) * half, half, 0)
    part = mine + lax.ppermute(theirs, "inner", [(i, i ^ 1) for i in range(size)])
    bit = 2
    while bit < size:
        part = part + lax.ppermute(part, "inner", [(i, i ^ bit) for i in range(size)])
        bit *= 2
    return part


def per_device(activations, out_grads, site_weights):
    sites = lax.axis_size("site")
    inner = lax.axis_size("inner")
    me = lax.axis_index("site")
    inputs = activations[0]
    grads = out_grads[0]
    count = inputs.shape[0]
    rows = grads.shape[1] // sites

    every_input = (site_gather(inputs.astype(f32) * 2.0) * 0.5).astype(bf16)
    core = lax.axis_index("inner") % 2
    split = inner % 2 == 0 and count % 16 == 0
    if split:
        own_rows = lax.dynamic_slice_in_dim(grads, core * (count // 2), count // 2, 0)
        wide = line_gather(own_rows.astype(f32) * 2.0)
        every_grad = halves(wide, lambda v: (v * 0.5).astype(bf16))
    else:
        every_grad = (site_gather(grads.astype(f32) * 2.0) * 0.5).astype(bf16)

    def mixed_of(left, pair):
        return exact_dot("tu,uc->tc", inputs, pair, exact_first=False) / (count * count) + damping * left / count

    def token_pair(left):
        return inner_sum(exact_dot("tc,uc->tu", inputs, left, exact_first=False), inner)

    def image_of(mixed_all):
        return exact_dot("std,stc->dc", every_grad, mixed_all)

    left_w = jnp.dot(grads, site_weights[0], preferred_element_type=f32)
    mixed_w = mixed_of(left_w, token_pair(left_w))
    mixed_w_all = site_gather(mixed_w)
    if split:
        half = count // 2
        turned = jnp.concatenate([mixed_w_all[:, half:], mixed_w_all[:, :half]], axis=1)
        mixed_w_all = jnp.where(core == 0, mixed_w_all, turned)
    rhs = image_of(mixed_w_all)

    def square_sum(x):
        return inner_sum(jnp.sum(x * x), inner)

    def pair_sum(left, scalar):
        partial = exact_dot("tc,uc->tu", inputs, left, exact_first=False)
        extra = jnp.full((8, count), scalar, f32)
        if not split:
            total = inner_sum(jnp.concatenate([partial, extra]), inner)
            return total[:count], total[count, 0]
        half = count // 2
        mine = jnp.concatenate([lax.dynamic_slice_in_dim(partial, core * half, half, 0), extra])
        theirs = jnp.concatenate([lax.dynamic_slice_in_dim(partial, (1 - core) * half, half, 0), extra])
        part = mine + lax.ppermute(theirs, "inner", [(i, i ^ 1) for i in range(inner)])
        bit = 2
        while bit < inner:
            part = part + lax.ppermute(part, "inner", [(i, i ^ bit) for i in range(inner)])
            bit *= 2
        return part[:half], part[half, 0]

    def pair_spread(pair_part):
        if not split:
            return site_gather(pair_part)
        return halves(site_gather(pair_part))

    def apply_operator(pair_part, direction):
        pair_all = pair_spread(pair_part)
        left_all = exact_dot("std,dc->stc", every_grad, direction)
        pair_all, left_all = lax.optimization_barrier((pair_all, left_all))
        mixed_all = (
            exact_dot("stu,suc->stc", every_input, pair_all, exact_first=False) / (count * count)
            + damping * left_all / count
        )
        return image_of(mixed_all)

    merged = jnp.zeros_like(rhs)
    residual = rhs
    direction = rhs
    pair_part, norm_now = pair_sum(exact_dot("td,dc->tc", grads, rhs), jnp.sum(rhs * rhs))
    for count_step in range(ITERS):
        if count_step:
            pair_r, norm_next = pair_sum(exact_dot("td,dc->tc", grads, residual), jnp.sum(residual * residual))
            beta = norm_next / norm_now
            pair_part = pair_r + beta * pair_part
            direction = residual + beta * direction
            norm_now = norm_next
        image = apply_operator(pair_part, direction)
        alpha = norm_now / inner_sum(jnp.sum(direction * image), inner)
        merged = merged + alpha * direction
        residual = residual - alpha * image
    norm_next = square_sum(residual)
    direction = residual + norm_next / norm_now * direction
    return lax.dynamic_slice_in_dim(merged, me * rows, rows, 0)


def solution(mesh):
    return jax.shard_map(
        per_device,
        mesh=mesh,
        in_specs=(
            P(("group", "site"), None, "inner"),
            P(("group", "site"), None, None),
            P(("group", "site"), None, "inner"),
        ),
        out_specs=P(("group", "site"), "inner"),
        check_vma=False,
    )
```

```python
import jax
import jax.numpy as jnp
from jax import lax
from jax.sharding import PartitionSpec as P

ITERS = 4

damping = 1.0
f32 = jnp.float32
bf16 = jnp.bfloat16


def pieces(x):
    hi = lax.reduce_precision(x, exponent_bits=8, mantissa_bits=7)
    rest = x - hi
    mid = lax.reduce_precision(rest, exponent_bits=8, mantissa_bits=7)
    lo = rest - mid
    return hi.astype(bf16), mid.astype(bf16), lo.astype(bf16)


def exact_dot(spec, exact, value, exact_first=True):
    hi, mid, lo = pieces(value)

    def one(part):
        if exact_first:
            return jnp.einsum(spec, exact, part, preferred_element_type=f32)
        return jnp.einsum(spec, part, exact, preferred_element_type=f32)

    return one(hi) + (one(mid) + one(lo))


def site_gather(x):
    return lax.optimization_barrier(lax.all_gather(lax.optimization_barrier(x), "site"))


def line_gather(x):
    sites = lax.axis_size("site")
    me = lax.axis_index("site")
    out = lax.dynamic_update_slice_in_dim(jnp.zeros((sites,) + x.shape, x.dtype), x[None], me, 0)
    right = left = x
    for step in range(1, sites):
        right = lax.ppermute(right, "site", [(i, i + 1) for i in range(sites - 1)])
        left = lax.ppermute(left, "site", [(i + 1, i) for i in range(sites - 1)])
        for block, at in ((right, (me - step) % sites), (left, (me + step) % sites)):
            now = lax.dynamic_index_in_dim(out, at, 0)
            out = lax.dynamic_update_slice_in_dim(out, now + block[None], at, 0)
    return out


def inner_sum(x, size):
    if size & (size - 1):
        return lax.psum(x, "inner")
    bit = 1
    while bit < size:
        x = x + lax.ppermute(x, "inner", [(i, i ^ bit) for i in range(size)])
        bit *= 2
    return x


def halves(x, finish=lambda v: v):
    other = lax.ppermute(x, "inner", [(i, i ^ 1) for i in range(lax.axis_size("inner"))])
    return jnp.concatenate([finish(x), finish(other)], axis=1)


def half_sum(x, size):
    core = lax.axis_index("inner") % 2
    half = x.shape[0] // 2
    mine = lax.dynamic_slice_in_dim(x, core * half, half, 0)
    theirs = lax.dynamic_slice_in_dim(x, (1 - core) * half, half, 0)
    part = mine + lax.ppermute(theirs, "inner", [(i, i ^ 1) for i in range(size)])
    bit = 2
    while bit < size:
        part = part + lax.ppermute(part, "inner", [(i, i ^ bit) for i in range(size)])
        bit *= 2
    return part


def per_device(activations, out_grads, site_weights):
    sites = lax.axis_size("site")
    inner = lax.axis_size("inner")
    me = lax.axis_index("site")
    inputs = activations[0]
    grads = out_grads[0]
    count = inputs.shape[0]
    rows = grads.shape[1] // sites

    core = lax.axis_index("inner") % 2
    split = inner % 2 == 0 and count % 16 == 0
    if split:
        own_rows = lax.dynamic_slice_in_dim(grads, core * (count // 2), count // 2, 0)
        wide = site_gather(own_rows.astype(f32) * 2.0)
        every_grad = halves(wide, lambda v: (v * 0.5).astype(bf16))
    else:
        every_grad = (site_gather(grads.astype(f32) * 2.0) * 0.5).astype(bf16)

    def mixed_of(left, pair):
        return exact_dot("tu,uc->tc", inputs, pair, exact_first=False) / (count * count) + damping * left / count

    def token_pair(left):
        return inner_sum(exact_dot("tc,uc->tu", inputs, left, exact_first=False), inner)

    def image_of(mixed_all):
        return exact_dot("std,stc->dc", every_grad, mixed_all)

    left_w = jnp.dot(grads, site_weights[0], preferred_element_type=f32)
    mixed_w = mixed_of(left_w, token_pair(left_w))
    mixed_w_all = site_gather(mixed_w)
    if split:
        half = count // 2
        turned = jnp.concatenate([mixed_w_all[:, half:], mixed_w_all[:, :half]], axis=1)
        mixed_w_all = jnp.where(core == 0, mixed_w_all, turned)
    rhs = image_of(mixed_w_all)
    wide_input, mixed_w_all = lax.optimization_barrier((inputs.astype(f32) * 2.0, mixed_w_all))
    every_input = (line_gather(wide_input) * 0.5).astype(bf16)

    def square_sum(x):
        return inner_sum(jnp.sum(x * x), inner)

    def pair_sum(left, scalar):
        partial = exact_dot("tc,uc->tu", inputs, left, exact_first=False)
        extra = jnp.full((8, count), scalar, f32)
        if not split:
            total = inner_sum(jnp.concatenate([partial, extra]), inner)
            return total[:count], total[count, 0]
        half = count // 2
        mine = jnp.concatenate([lax.dynamic_slice_in_dim(partial, core * half, half, 0), extra])
        theirs = jnp.concatenate([lax.dynamic_slice_in_dim(partial, (1 - core) * half, half, 0), extra])
        part = mine + lax.ppermute(theirs, "inner", [(i, i ^ 1) for i in range(inner)])
        bit = 2
        while bit < inner:
            part = part + lax.ppermute(part, "inner", [(i, i ^ bit) for i in range(inner)])
            bit *= 2
        return part[:half], part[half, 0]

    def pair_spread(pair_part):
        if not split:
            return site_gather(pair_part)
        return halves(site_gather(pair_part))

    def apply_operator(pair_part, direction):
        pair_all = pair_spread(pair_part)
        left_all = exact_dot("std,dc->stc", every_grad, direction)
        pair_all, left_all = lax.optimization_barrier((pair_all, left_all))
        mixed_all = (
            exact_dot("stu,suc->stc", every_input, pair_all, exact_first=False) / (count * count)
            + damping * left_all / count
        )
        return image_of(mixed_all)

    merged = jnp.zeros_like(rhs)
    residual = rhs
    direction = rhs
    pair_part, norm_now = pair_sum(exact_dot("td,dc->tc", grads, rhs), jnp.sum(rhs * rhs))
    for count_step in range(ITERS):
        if count_step:
            pair_r, norm_next = pair_sum(exact_dot("td,dc->tc", grads, residual), jnp.sum(residual * residual))
            beta = norm_next / norm_now
            pair_part = pair_r + beta * pair_part
            direction = residual + beta * direction
            norm_now = norm_next
        image = apply_operator(pair_part, direction)
        alpha = norm_now / inner_sum(jnp.sum(direction * image), inner)
        merged = merged + alpha * direction
        residual = residual - alpha * image
    norm_next = square_sum(residual)
    direction = residual + norm_next / norm_now * direction
    return lax.dynamic_slice_in_dim(merged, me * rows, rows, 0)


def solution(mesh):
    return jax.shard_map(
        per_device,
        mesh=mesh,
        in_specs=(
            P(("group", "site"), None, "inner"),
            P(("group", "site"), None, None),
            P(("group", "site"), None, "inner"),
        ),
        out_specs=P(("group", "site"), "inner"),
        check_vma=False,
    )
```

```python
import jax
import jax.numpy as jnp
from jax import lax
from jax.sharding import PartitionSpec as P

ITERS = 4

damping = 1.0
f32 = jnp.float32
bf16 = jnp.bfloat16


def pieces(x):
    hi = lax.reduce_precision(x, exponent_bits=8, mantissa_bits=7)
    rest = x - hi
    mid = lax.reduce_precision(rest, exponent_bits=8, mantissa_bits=7)
    lo = rest - mid
    return hi.astype(bf16), mid.astype(bf16), lo.astype(bf16)


def exact_dot(spec, exact, value, exact_first=True):
    hi, mid, lo = pieces(value)

    def one(part):
        if exact_first:
            return jnp.einsum(spec, exact, part, preferred_element_type=f32)
        return jnp.einsum(spec, part, exact, preferred_element_type=f32)

    return one(hi) + (one(mid) + one(lo))


def site_gather(x):
    return lax.optimization_barrier(lax.all_gather(lax.optimization_barrier(x), "site"))


def line_gather(x):
    sites = lax.axis_size("site")
    me = lax.axis_index("site")
    out = lax.dynamic_update_slice_in_dim(jnp.zeros((sites,) + x.shape, x.dtype), x[None], me, 0)
    right = left = x
    steps = sites
    if sites == 4:
        far = lax.ppermute(x, "site", [(0, 3), (3, 0)])
        now = lax.dynamic_index_in_dim(out, 3 - me, 0)
        out = lax.dynamic_update_slice_in_dim(out, now + far[None], 3 - me, 0)
        steps = 3
    for step in range(1, steps):
        right = lax.ppermute(right, "site", [(i, i + 1) for i in range(sites - 1)])
        left = lax.ppermute(left, "site", [(i + 1, i) for i in range(sites - 1)])
        for block, at in ((right, (me - step) % sites), (left, (me + step) % sites)):
            now = lax.dynamic_index_in_dim(out, at, 0)
            out = lax.dynamic_update_slice_in_dim(out, now + block[None], at, 0)
    return out


def inner_sum(x, size):
    if size & (size - 1):
        return lax.psum(x, "inner")
    bit = 1
    while bit < size:
        x = x + lax.ppermute(x, "inner", [(i, i ^ bit) for i in range(size)])
        bit *= 2
    return x


def halves(x, finish=lambda v: v):
    other = lax.ppermute(x, "inner", [(i, i ^ 1) for i in range(lax.axis_size("inner"))])
    return jnp.concatenate([finish(x), finish(other)], axis=1)


def half_sum(x, size):
    core = lax.axis_index("inner") % 2
    half = x.shape[0] // 2
    mine = lax.dynamic_slice_in_dim(x, core * half, half, 0)
    theirs = lax.dynamic_slice_in_dim(x, (1 - core) * half, half, 0)
    part = mine + lax.ppermute(theirs, "inner", [(i, i ^ 1) for i in range(size)])
    bit = 2
    while bit < size:
        part = part + lax.ppermute(part, "inner", [(i, i ^ bit) for i in range(size)])
        bit *= 2
    return part


def per_device(activations, out_grads, site_weights):
    sites = lax.axis_size("site")
    inner = lax.axis_size("inner")
    me = lax.axis_index("site")
    inputs = activations[0]
    grads = out_grads[0]
    count = inputs.shape[0]
    rows = grads.shape[1] // sites

    core = lax.axis_index("inner") % 2
    split = inner % 2 == 0 and count % 16 == 0
    if split:
        own_rows = lax.dynamic_slice_in_dim(grads, core * (count // 2), count // 2, 0)
        wide = site_gather(own_rows.astype(f32) * 2.0)
        every_grad = halves(wide, lambda v: (v * 0.5).astype(bf16))
    else:
        every_grad = (site_gather(grads.astype(f32) * 2.0) * 0.5).astype(bf16)

    def mixed_of(left, pair):
        return exact_dot("tu,uc->tc", inputs, pair, exact_first=False) / (count * count) + damping * left / count

    def token_pair(left):
        return inner_sum(exact_dot("tc,uc->tu", inputs, left, exact_first=False), inner)

    def image_of(mixed_all):
        return exact_dot("std,stc->dc", every_grad, mixed_all)

    left_w = jnp.dot(grads, site_weights[0], preferred_element_type=f32)
    mixed_w = mixed_of(left_w, token_pair(left_w))
    mixed_w_all = site_gather(mixed_w)
    if split:
        half = count // 2
        turned = jnp.concatenate([mixed_w_all[:, half:], mixed_w_all[:, :half]], axis=1)
        mixed_w_all = jnp.where(core == 0, mixed_w_all, turned)
    rhs = image_of(mixed_w_all)
    wide_input, mixed_w_all = lax.optimization_barrier((inputs.astype(f32) * 2.0, mixed_w_all))
    every_input = (line_gather(wide_input) * 0.5).astype(bf16)

    def square_sum(x):
        return inner_sum(jnp.sum(x * x), inner)

    def pair_sum(left, scalar):
        partial = exact_dot("tc,uc->tu", inputs, left, exact_first=False)
        extra = jnp.full((8, count), scalar, f32)
        if not split:
            total = inner_sum(jnp.concatenate([partial, extra]), inner)
            return total[:count], total[count, 0]
        half = count // 2
        mine = jnp.concatenate([lax.dynamic_slice_in_dim(partial, core * half, half, 0), extra])
        theirs = jnp.concatenate([lax.dynamic_slice_in_dim(partial, (1 - core) * half, half, 0), extra])
        part = mine + lax.ppermute(theirs, "inner", [(i, i ^ 1) for i in range(inner)])
        bit = 2
        while bit < inner:
            part = part + lax.ppermute(part, "inner", [(i, i ^ bit) for i in range(inner)])
            bit *= 2
        return part[:half], part[half, 0]

    def pair_spread(pair_part):
        if not split:
            return site_gather(pair_part)
        return halves(site_gather(pair_part))

    def apply_operator(pair_part, direction):
        pair_all = pair_spread(pair_part)
        left_all = exact_dot("std,dc->stc", every_grad, direction)
        pair_all, left_all = lax.optimization_barrier((pair_all, left_all))
        mixed_all = (
            exact_dot("stu,suc->stc", every_input, pair_all, exact_first=False) / (count * count)
            + damping * left_all / count
        )
        return image_of(mixed_all)

    merged = jnp.zeros_like(rhs)
    residual = rhs
    direction = rhs
    pair_part, norm_now = pair_sum(exact_dot("td,dc->tc", grads, rhs), jnp.sum(rhs * rhs))
    for count_step in range(ITERS):
        if count_step:
            pair_r, norm_next = pair_sum(exact_dot("td,dc->tc", grads, residual), jnp.sum(residual * residual))
            beta = norm_next / norm_now
            pair_part = pair_r + beta * pair_part
            direction = residual + beta * direction
            norm_now = norm_next
        image = apply_operator(pair_part, direction)
        alpha = norm_now / inner_sum(jnp.sum(direction * image), inner)
        merged = merged + alpha * direction
        residual = residual - alpha * image
    norm_next = square_sum(residual)
    direction = residual + norm_next / norm_now * direction
    return lax.dynamic_slice_in_dim(merged, me * rows, rows, 0)


def solution(mesh):
    return jax.shard_map(
        per_device,
        mesh=mesh,
        in_specs=(
            P(("group", "site"), None, "inner"),
            P(("group", "site"), None, None),
            P(("group", "site"), None, "inner"),
        ),
        out_specs=P(("group", "site"), "inner"),
        check_vma=False,
    )
```

```python
import jax
import jax.numpy as jnp
from jax import lax
from jax.sharding import PartitionSpec as P

ITERS = 4

damping = 1.0
f32 = jnp.float32
bf16 = jnp.bfloat16


def pieces(x):
    hi = lax.reduce_precision(x, exponent_bits=8, mantissa_bits=7)
    rest = x - hi
    mid = lax.reduce_precision(rest, exponent_bits=8, mantissa_bits=7)
    lo = rest - mid
    return hi.astype(bf16), mid.astype(bf16), lo.astype(bf16)


def exact_dot(spec, exact, value, exact_first=True):
    hi, mid, lo = pieces(value)

    def one(part):
        if exact_first:
            return jnp.einsum(spec, exact, part, preferred_element_type=f32)
        return jnp.einsum(spec, part, exact, preferred_element_type=f32)

    return one(hi) + (one(mid) + one(lo))


def site_gather(x):
    return lax.optimization_barrier(lax.all_gather(lax.optimization_barrier(x), "site"))


def line_gather(x):
    sites = lax.axis_size("site")
    me = lax.axis_index("site")
    out = lax.dynamic_update_slice_in_dim(jnp.zeros((sites,) + x.shape, x.dtype), x[None], me, 0)
    right = left = x
    steps = sites
    if sites == 4:
        far = lax.ppermute(x, "site", [(0, 3), (3, 0)])
        now = lax.dynamic_index_in_dim(out, 3 - me, 0)
        out = lax.dynamic_update_slice_in_dim(out, now + far[None], 3 - me, 0)
        steps = 3
    for step in range(1, steps):
        right = lax.ppermute(right, "site", [(i, i + 1) for i in range(sites - 1)])
        left = lax.ppermute(left, "site", [(i + 1, i) for i in range(sites - 1)])
        for block, at in ((right, (me - step) % sites), (left, (me + step) % sites)):
            now = lax.dynamic_index_in_dim(out, at, 0)
            out = lax.dynamic_update_slice_in_dim(out, now + block[None], at, 0)
    return out


def inner_sum(x, size):
    if size & (size - 1):
        return lax.psum(x, "inner")
    bit = 1
    while bit < size:
        x = x + lax.ppermute(x, "inner", [(i, i ^ bit) for i in range(size)])
        bit *= 2
    return x


def halves(x, finish=lambda v: v):
    other = lax.ppermute(x, "inner", [(i, i ^ 1) for i in range(lax.axis_size("inner"))])
    return jnp.concatenate([finish(x), finish(other)], axis=1)


def half_sum(x, size):
    core = lax.axis_index("inner") % 2
    half = x.shape[0] // 2
    mine = lax.dynamic_slice_in_dim(x, core * half, half, 0)
    theirs = lax.dynamic_slice_in_dim(x, (1 - core) * half, half, 0)
    part = mine + lax.ppermute(theirs, "inner", [(i, i ^ 1) for i in range(size)])
    bit = 2
    while bit < size:
        part = part + lax.ppermute(part, "inner", [(i, i ^ bit) for i in range(size)])
        bit *= 2
    return part


def per_device(activations, out_grads, site_weights):
    sites = lax.axis_size("site")
    inner = lax.axis_size("inner")
    me = lax.axis_index("site")
    inputs = activations[0]
    grads = out_grads[0]
    count = inputs.shape[0]
    rows = grads.shape[1] // sites

    core = lax.axis_index("inner") % 2
    split = inner % 2 == 0 and count % 16 == 0
    if split:
        own_rows = lax.dynamic_slice_in_dim(grads, core * (count // 2), count // 2, 0)
        wide = site_gather(own_rows.astype(f32) * 2.0)
        every_grad = halves(wide, lambda v: (v * 0.5).astype(bf16))
    else:
        every_grad = (site_gather(grads.astype(f32) * 2.0) * 0.5).astype(bf16)

    def mixed_of(left, pair):
        return exact_dot("tu,uc->tc", inputs, pair, exact_first=False) / (count * count) + damping * left / count

    def token_pair(left):
        return inner_sum(exact_dot("tc,uc->tu", inputs, left, exact_first=False), inner)

    def image_of(mixed_all):
        return exact_dot("std,stc->dc", every_grad, mixed_all)

    left_w = jnp.dot(grads, site_weights[0], preferred_element_type=f32)
    mixed_w = mixed_of(left_w, token_pair(left_w))
    mixed_w_all = site_gather(mixed_w)
    if split:
        half = count // 2
        turned = jnp.concatenate([mixed_w_all[:, half:], mixed_w_all[:, :half]], axis=1)
        mixed_w_all = jnp.where(core == 0, mixed_w_all, turned)
    rhs = image_of(mixed_w_all)
    wide_input, mixed_w_all = lax.optimization_barrier((inputs.astype(f32) * 2.0, mixed_w_all))
    every_input = (line_gather(wide_input) * 0.5).astype(bf16)

    def square_sum(x):
        return inner_sum(jnp.sum(x * x), inner)

    def pair_sum(left, scalar):
        partial = exact_dot("tc,uc->tu", inputs, left, exact_first=False)
        extra = jnp.full((8, count), scalar, f32)
        if not split:
            total = inner_sum(jnp.concatenate([partial, extra]), inner)
            return total[:count], total[count, 0]
        half = count // 2
        mine = jnp.concatenate([lax.dynamic_slice_in_dim(partial, core * half, half, 0), extra])
        theirs = jnp.concatenate([lax.dynamic_slice_in_dim(partial, (1 - core) * half, half, 0), extra])
        part = mine + lax.ppermute(theirs, "inner", [(i, i ^ 1) for i in range(inner)])
        bit = 2
        while bit < inner:
            part = part + lax.ppermute(part, "inner", [(i, i ^ bit) for i in range(inner)])
            bit *= 2
        return part[:half], part[half, 0]

    def pair_spread(pair_part):
        if not split:
            return site_gather(pair_part)
        if sites <= 4:
            return halves(line_gather(pair_part))
        return halves(site_gather(pair_part))

    def apply_operator(pair_part, direction):
        pair_all = pair_spread(pair_part)
        left_all = exact_dot("std,dc->stc", every_grad, direction)
        pair_all, left_all = lax.optimization_barrier((pair_all, left_all))
        mixed_all = (
            exact_dot("stu,suc->stc", every_input, pair_all, exact_first=False) / (count * count)
            + damping * left_all / count
        )
        return image_of(mixed_all)

    merged = jnp.zeros_like(rhs)
    residual = rhs
    direction = rhs
    pair_part, norm_now = pair_sum(exact_dot("td,dc->tc", grads, rhs), jnp.sum(rhs * rhs))
    for count_step in range(ITERS):
        if count_step:
            pair_r, norm_next = pair_sum(exact_dot("td,dc->tc", grads, residual), jnp.sum(residual * residual))
            beta = norm_next / norm_now
            pair_part = pair_r + beta * pair_part
            direction = residual + beta * direction
            norm_now = norm_next
        image = apply_operator(pair_part, direction)
        alpha = norm_now / inner_sum(jnp.sum(direction * image), inner)
        merged = merged + alpha * direction
        residual = residual - alpha * image
    norm_next = square_sum(residual)
    direction = residual + norm_next / norm_now * direction
    return lax.dynamic_slice_in_dim(merged, me * rows, rows, 0)


def solution(mesh):
    return jax.shard_map(
        per_device,
        mesh=mesh,
        in_specs=(
            P(("group", "site"), None, "inner"),
            P(("group", "site"), None, None),
            P(("group", "site"), None, "inner"),
        ),
        out_specs=P(("group", "site"), "inner"),
        check_vma=False,
    )
```

```python
import jax
import jax.numpy as jnp
from jax import lax
from jax.sharding import PartitionSpec as P

ITERS = 4

damping = 1.0
f32 = jnp.float32
bf16 = jnp.bfloat16


def pieces(x):
    hi = lax.reduce_precision(x, exponent_bits=8, mantissa_bits=7)
    rest = x - hi
    mid = lax.reduce_precision(rest, exponent_bits=8, mantissa_bits=7)
    lo = rest - mid
    return hi.astype(bf16), mid.astype(bf16), lo.astype(bf16)


def exact_dot(spec, exact, value, exact_first=True):
    hi, mid, lo = pieces(value)

    def one(part):
        if exact_first:
            return jnp.einsum(spec, exact, part, preferred_element_type=f32)
        return jnp.einsum(spec, part, exact, preferred_element_type=f32)

    return one(hi) + (one(mid) + one(lo))


def site_gather(x):
    return lax.optimization_barrier(lax.all_gather(lax.optimization_barrier(x), "site"))


def line_gather(x):
    sites = lax.axis_size("site")
    me = lax.axis_index("site")
    out = lax.dynamic_update_slice_in_dim(jnp.zeros((sites,) + x.shape, x.dtype), x[None], me, 0)
    right = left = x
    steps = sites
    if sites == 4:
        far = lax.ppermute(x, "site", [(0, 3), (3, 0)])
        now = lax.dynamic_index_in_dim(out, 3 - me, 0)
        out = lax.dynamic_update_slice_in_dim(out, now + far[None], 3 - me, 0)
        steps = 3
    for step in range(1, steps):
        right = lax.ppermute(right, "site", [(i, i + 1) for i in range(sites - 1)])
        left = lax.ppermute(left, "site", [(i + 1, i) for i in range(sites - 1)])
        for block, at in ((right, (me - step) % sites), (left, (me + step) % sites)):
            now = lax.dynamic_index_in_dim(out, at, 0)
            out = lax.dynamic_update_slice_in_dim(out, now + block[None], at, 0)
    return out


def inner_sum(x, size):
    if size & (size - 1):
        return lax.psum(x, "inner")
    bit = 1
    while bit < size:
        x = x + lax.ppermute(x, "inner", [(i, i ^ bit) for i in range(size)])
        bit *= 2
    return x


def halves(x, finish=lambda v: v):
    other = lax.ppermute(x, "inner", [(i, i ^ 1) for i in range(lax.axis_size("inner"))])
    return jnp.concatenate([finish(x), finish(other)], axis=1)


def half_sum(x, size):
    core = lax.axis_index("inner") % 2
    half = x.shape[0] // 2
    mine = lax.dynamic_slice_in_dim(x, core * half, half, 0)
    theirs = lax.dynamic_slice_in_dim(x, (1 - core) * half, half, 0)
    part = mine + lax.ppermute(theirs, "inner", [(i, i ^ 1) for i in range(size)])
    bit = 2
    while bit < size:
        part = part + lax.ppermute(part, "inner", [(i, i ^ bit) for i in range(size)])
        bit *= 2
    return part


def per_device(activations, out_grads, site_weights):
    sites = lax.axis_size("site")
    inner = lax.axis_size("inner")
    me = lax.axis_index("site")
    inputs = activations[0]
    grads = out_grads[0]
    count = inputs.shape[0]
    rows = grads.shape[1] // sites

    core = lax.axis_index("inner") % 2
    split = inner % 2 == 0 and count % 16 == 0
    if split:
        own_rows = lax.dynamic_slice_in_dim(grads, core * (count // 2), count // 2, 0)
        wide = site_gather(own_rows.astype(f32) * 2.0)
        every_grad = halves(wide, lambda v: (v * 0.5).astype(bf16))
    else:
        every_grad = (site_gather(grads.astype(f32) * 2.0) * 0.5).astype(bf16)

    def mixed_of(left, pair):
        return exact_dot("tu,uc->tc", inputs, pair, exact_first=False) / (count * count) + damping * left / count

    def token_pair(left):
        return inner_sum(exact_dot("tc,uc->tu", inputs, left, exact_first=False), inner)

    def image_of(mixed_all):
        return exact_dot("std,stc->dc", every_grad, mixed_all)

    left_w = jnp.dot(grads, site_weights[0], preferred_element_type=f32)
    mixed_w = mixed_of(left_w, token_pair(left_w))
    mixed_w_all = line_gather(mixed_w) if sites <= 4 else site_gather(mixed_w)
    if split:
        half = count // 2
        turned = jnp.concatenate([mixed_w_all[:, half:], mixed_w_all[:, :half]], axis=1)
        mixed_w_all = jnp.where(core == 0, mixed_w_all, turned)
    rhs = image_of(mixed_w_all)
    wide_input, mixed_w_all = lax.optimization_barrier((inputs.astype(f32) * 2.0, mixed_w_all))
    every_input = (line_gather(wide_input) * 0.5).astype(bf16)

    def square_sum(x):
        return inner_sum(jnp.sum(x * x), inner)

    def pair_sum(left, scalar):
        partial = exact_dot("tc,uc->tu", inputs, left, exact_first=False)
        extra = jnp.full((8, count), scalar, f32)
        if not split:
            total = inner_sum(jnp.concatenate([partial, extra]), inner)
            return total[:count], total[count, 0]
        half = count // 2
        mine = jnp.concatenate([lax.dynamic_slice_in_dim(partial, core * half, half, 0), extra])
        theirs = jnp.concatenate([lax.dynamic_slice_in_dim(partial, (1 - core) * half, half, 0), extra])
        part = mine + lax.ppermute(theirs, "inner", [(i, i ^ 1) for i in range(inner)])
        bit = 2
        while bit < inner:
            part = part + lax.ppermute(part, "inner", [(i, i ^ bit) for i in range(inner)])
            bit *= 2
        return part[:half], part[half, 0]

    def pair_spread(pair_part):
        if not split:
            return site_gather(pair_part)
        if sites <= 4:
            return halves(line_gather(pair_part))
        return halves(site_gather(pair_part))

    def apply_operator(pair_part, direction):
        pair_all = pair_spread(pair_part)
        left_all = exact_dot("std,dc->stc", every_grad, direction)
        pair_all, left_all = lax.optimization_barrier((pair_all, left_all))
        mixed_all = (
            exact_dot("stu,suc->stc", every_input, pair_all, exact_first=False) / (count * count)
            + damping * left_all / count
        )
        return image_of(mixed_all)

    merged = jnp.zeros_like(rhs)
    residual = rhs
    direction = rhs
    pair_part, norm_now = pair_sum(exact_dot("td,dc->tc", grads, rhs), jnp.sum(rhs * rhs))
    for count_step in range(ITERS):
        if count_step:
            pair_r, norm_next = pair_sum(exact_dot("td,dc->tc", grads, residual), jnp.sum(residual * residual))
            beta = norm_next / norm_now
            pair_part = pair_r + beta * pair_part
            direction = residual + beta * direction
            norm_now = norm_next
        image = apply_operator(pair_part, direction)
        alpha = norm_now / inner_sum(jnp.sum(direction * image), inner)
        merged = merged + alpha * direction
        residual = residual - alpha * image
    norm_next = square_sum(residual)
    direction = residual + norm_next / norm_now * direction
    return lax.dynamic_slice_in_dim(merged, me * rows, rows, 0)


def solution(mesh):
    return jax.shard_map(
        per_device,
        mesh=mesh,
        in_specs=(
            P(("group", "site"), None, "inner"),
            P(("group", "site"), None, None),
            P(("group", "site"), None, "inner"),
        ),
        out_specs=P(("group", "site"), "inner"),
        check_vma=False,
    )
```
